128 devices in a mesh: row: 8 (over z, x_hi), col: 16 (over x_lo, y, core).
Axes of the slice: x: 4 (x_hi: 2, x_lo: 2; x = x_hi * 2 + x_lo), y: 4, z: 4, core: 2. Of those that a mesh axis runs over, the one named last changes fastest.
Arguments:
- tokens: bfloat16 [512, 8192], P('row', 'col'), may hold values from -6 to 6
- gate_weight: bfloat16 [8192, 28672], P('col', 'row'), may hold values from -0.09375 to 0.09375
- up_weight: bfloat16 [8192, 28672], P('col', 'row'), may hold values from -0.09375 to 0.09375
- down_weight: bfloat16 [28672, 8192], P('row', 'col'), may hold values from -0.046875 to 0.046875
- gate_keep: int32 [64, 224], P('col', 'row'), may hold values from 0 to 1, as said below
- up_keep: int32 [64, 224], P('col', 'row'), may hold values from 0 to 1, as said below
- down_keep: int32 [224, 64], P('row', 'col'), may hold values from 0 to 1, as said below
Outputs:
- mixed: bfloat16 [512, 8192], P('row', 'col')
The draws below stay inside these ranges and needn't reach their ends.
Inputs may be any that keep to these rules, and one draw needn't show every extreme that they name: `gate_keep`: 1 keeps the block, 0 drops it; the kept share differs between regions of blocks. `up_keep`: 1 keeps the block, 0 drops it; the kept share differs between regions of blocks. `down_keep`: 1 keeps the block, 0 drops it; the kept share differs between regions of blocks.
All inputs are finite; a program needn't handle non-finite values.
Results may differ from the reference program's by a relative error of at most 0.0049.
Values may be sent and summed in bfloat16 or wider, within the bound.
No kernel may reach another device: no remote copies, remote signals or barrier semaphores. Data moves between devices by JAX's collectives and lax.ppermute only.
A program may use at most 128 MiB of HBM per device.

```python
import jax
import jax.numpy as jnp

D = 8192
FF = 28672
BLOCK = 128
TOKENS = 512


def keep_blocks(key, rows, cols):
    coarse_rows = (rows + 7) // 8
    coarse_cols = (cols + 7) // 8
    level = jax.random.randint(jax.random.fold_in(key, 11), (coarse_rows, coarse_cols), 1, 8)
    level = jnp.repeat(jnp.repeat(level, 8, axis=0), 8, axis=1)[:rows, :cols]
    values = jax.random.randint(jax.random.fold_in(key, 12), (rows, cols), 0, 8)
    return (values < level).astype(jnp.int32)


def draw_gate_keep(key, part):
    return keep_blocks(jax.random.fold_in(key, 1), D // BLOCK, FF // BLOCK)


def draw_up_keep(key, part):
    return keep_blocks(jax.random.fold_in(key, 2), D // BLOCK, FF // BLOCK)


def draw_down_keep(key, part):
    return keep_blocks(jax.random.fold_in(key, 3), FF // BLOCK, D // BLOCK)


def shard_levels(key, extent, shards, smallest, largest):
    gain, own = 1.0, jax.random.fold_in(key, 6)
    for dim, blocks in shards:
        heights = jnp.exp(jax.random.uniform(jax.random.fold_in(own, dim), (blocks,), jnp.float32, smallest / len(shards), largest / len(shards)))
        gain = gain * jnp.repeat(heights, extent[dim] // blocks).reshape([-1 if axis == dim else 1 for axis in range(len(extent))])
    return gain


def scatter_about(key, extent, width, most, shards=(), held_as=jnp.bfloat16):
    entries = jax.random.normal(key, extent, jnp.float32) * width
    if len(shards) > 0:
        entries = shard_levels(key, extent, shards, -0.22, 0.18) * entries
    return jnp.clip(entries, min=-most, max=most).astype(held_as)


def setup_inputs(seed: int = 0) -> dict:
    key_list = jax.random.split(jax.random.key(seed), 8)
    return {
        "tokens": scatter_about(key_list[0], (TOKENS, D), 1.0, 6.0, ((0, 8), (1, 16))),
        "gate_weight": scatter_about(key_list[1], (D, FF), (D // 2) ** -0.5, 0.09375, ((0, 16), (1, 8))),
        "up_weight": scatter_about(key_list[2], (D, FF), (D // 2) ** -0.5, 0.09375, ((0, 16), (1, 8))),
        "down_weight": scatter_about(key_list[3], (FF, D), (FF // 2) ** -0.5, 0.046875, ((0, 8), (1, 16))),
        "gate_keep": draw_gate_keep(jax.random.fold_in(key_list[7], 71), 0),
        "up_keep": draw_up_keep(jax.random.fold_in(key_list[7], 71), 0),
        "down_keep": draw_down_keep(jax.random.fold_in(key_list[7], 71), 0),
    }


def expand(weight, keep):
    nrow, ncol = keep.shape
    rows, cols = weight.shape
    masked = weight.reshape(nrow, rows // nrow, ncol, cols // ncol) * keep.astype(jnp.bfloat16)[:, None, :, None]
    return masked.reshape(rows, cols)


def reference(tokens, gate_weight, up_weight, down_weight, gate_keep, up_keep, down_keep):
    gate = jnp.dot(tokens, expand(gate_weight, gate_keep), preferred_element_type=jnp.float32)
    up = jnp.dot(tokens, expand(up_weight, up_keep), preferred_element_type=jnp.float32)
    hidden = (jax.nn.silu(gate) * up).astype(jnp.bfloat16)
    return jnp.dot(hidden, expand(down_weight, down_keep), preferred_element_type=jnp.float32).astype(jnp.bfloat16)
```

```python
import jax
import jax.numpy as jnp
from jax import lax
from jax.sharding import PartitionSpec as P


def expand(weight, keep):
    nrow, ncol = keep.shape
    rows, cols = weight.shape
    masked = (
        weight.reshape(nrow, rows // nrow, ncol, cols // ncol)
        * keep.astype(jnp.bfloat16)[:, None, :, None]
    )
    return masked.reshape(rows, cols)


def on_device(tokens, gate_weight, up_weight, down_weight, gate_keep, up_keep, down_keep):
    hidden_cols = gate_weight.shape[1]
    features = lax.all_gather(tokens, "row", axis=0, tiled=True)
    pg = jnp.dot(features, expand(gate_weight, gate_keep), preferred_element_type=jnp.float32)
    pu = jnp.dot(features, expand(up_weight, up_keep), preferred_element_type=jnp.float32)
    pair = jnp.concatenate([pg, pu], axis=1)
    summed = lax.psum_scatter(pair, "col", scatter_dimension=0, tiled=True)
    hidden = (jax.nn.silu(summed[:, :hidden_cols]) * summed[:, hidden_cols:]).astype(jnp.bfloat16)
    hidden_all = lax.all_gather(hidden, "col", axis=0, tiled=True)
    partial_out = jnp.dot(
        hidden_all, expand(down_weight, down_keep), preferred_element_type=jnp.float32
    )
    return lax.psum_scatter(partial_out, "row", scatter_dimension=0, tiled=True).astype(
        jnp.bfloat16
    )


def solution(mesh):
    placed = (
        P("row", "col"),
        P("col", "row"),
        P("col", "row"),
        P("row", "col"),
        P("col", "row"),
        P("col", "row"),
        P("row", "col"),
    )
    return jax.shard_map(
        on_device, mesh=mesh, in_specs=placed, out_specs=P("row", "col"), check_vma=False
    )
```

```python
import jax
import jax.numpy as jnp
from jax import lax
from jax.sharding import Mesh
from jax.sharding import PartitionSpec as P

ROW = ("z", "x_hi")
COL = ("x_lo", "y", "core")
CHIPS = ("x_lo", "y")


def expand(weight, keep):
    nrow, ncol = keep.shape
    rows, cols = weight.shape
    masked = (
        weight.reshape(nrow, rows // nrow, ncol, cols // ncol)
        * keep.astype(jnp.bfloat16)[:, None, :, None]
    )
    return masked.reshape(rows, cols)


def on_device(tokens, gate_weight, up_weight, down_weight, gate_keep, up_keep, down_keep):
    hidden_cols = gate_weight.shape[1]
    features = lax.all_gather(tokens, ROW, axis=0, tiled=True)
    pg = jnp.dot(features, expand(gate_weight, gate_keep), preferred_element_type=jnp.float32)
    pu = jnp.dot(features, expand(up_weight, up_keep), preferred_element_type=jnp.float32)
    pair = jnp.concatenate([pg, pu], axis=1)
    on_chip = lax.psum_scatter(pair, "core", scatter_dimension=0, tiled=True)
    summed = lax.psum_scatter(on_chip, CHIPS, scatter_dimension=0, tiled=True)
    hidden = (jax.nn.silu(summed[:, :hidden_cols]) * summed[:, hidden_cols:]).astype(jnp.bfloat16)
    hidden_chip = lax.all_gather(hidden, CHIPS, axis=0, tiled=True)
    hidden_all = lax.all_gather(hidden_chip, "core", axis=0, tiled=True)
    partial_out = jnp.dot(
        hidden_all, expand(down_weight, down_keep), preferred_element_type=jnp.float32
    )
    n_row = partial_out.shape[0] // tokens.shape[0]
    pieces = partial_out.reshape(n_row, tokens.shape[0], partial_out.shape[1])
    pieces = lax.all_to_all(pieces, ROW, 0, 0, tiled=True)
    return jnp.sum(pieces, axis=0).astype(jnp.bfloat16)


def solution(mesh):
    fine = Mesh(mesh.devices.reshape(4, 2, 2, 4, 2), ROW + COL)
    placed = (
        P(ROW, COL),
        P(COL, ROW),
        P(COL, ROW),
        P(ROW, COL),
        P(COL, ROW),
        P(COL, ROW),
        P(ROW, COL),
    )
    return jax.shard_map(
        on_device, mesh=fine, in_specs=placed, out_specs=P(ROW, COL), check_vma=False
    )
```

```python
import jax
import jax.numpy as jnp
from jax import lax
from jax.sharding import Mesh
from jax.sharding import PartitionSpec as P

ROW = ("z", "x_hi")
COL = ("x_lo", "y", "core")


def expand(weight, keep):
    nrow, ncol = keep.shape
    rows, cols = weight.shape
    masked = (
        weight.reshape(nrow, rows // nrow, ncol, cols // ncol)
        * keep.astype(jnp.bfloat16)[:, None, :, None]
    )
    return masked.reshape(rows, cols)


def shift(x, k, n):
    return lax.ppermute(x, ROW, [(i, (i + k) % n) for i in range(n)])


def on_device(tokens, gate_weight, up_weight, down_weight, gate_keep, up_keep, down_keep):
    n = lax.axis_size(ROW)
    hidden_cols = gate_weight.shape[1]
    features = jnp.concatenate([tokens] + [shift(tokens, k, n) for k in range(1, n)], axis=0)
    pg = jnp.dot(features, expand(gate_weight, gate_keep), preferred_element_type=jnp.float32)
    pu = jnp.dot(features, expand(up_weight, up_keep), preferred_element_type=jnp.float32)
    pair = jnp.concatenate([pg, pu], axis=1)
    summed = lax.psum_scatter(pair, COL, scatter_dimension=0, tiled=True)
    hidden = (jax.nn.silu(summed[:, :hidden_cols]) * summed[:, hidden_cols:]).astype(jnp.bfloat16)
    hidden_all = lax.all_gather(hidden, COL, axis=0, tiled=True)
    partial_out = jnp.dot(
        hidden_all, expand(down_weight, down_keep), preferred_element_type=jnp.float32
    )
    t = tokens.shape[0]
    total = partial_out[:t]
    for k in range(1, n):
        total = total + shift(partial_out[k * t:(k + 1) * t], -k, n)
    return total.astype(jnp.bfloat16)


def solution(mesh):
    fine = Mesh(mesh.devices.reshape(4, 2, 2, 4, 2), ROW + COL)
    placed = (
        P(ROW, COL),
        P(COL, ROW),
        P(COL, ROW),
        P(ROW, COL),
        P(COL, ROW),
        P(COL, ROW),
        P(ROW, COL),
    )
    return jax.shard_map(
        on_device, mesh=fine, in_specs=placed, out_specs=P(ROW, COL), check_vma=False
    )
```

```python
import functools

import jax
import jax.numpy as jnp
from jax import lax
from jax.experimental import pallas as pl
from jax.experimental.pallas import tpu as pltpu
from jax.sharding import Mesh
from jax.sharding import PartitionSpec as P

BLOCK = 128
TILE = 256


def _gate_up_kernel(n_half, n_feat, gk_ref, uk_ref, x_ref, gw_ref, uw_ref, o_ref, w_scr):
    j = pl.program_id(0)

    def build(w_ref, k_ref, jj):
        for kb in range(n_feat):
            for hb in range(TILE // BLOCK):
                k = k_ref[kb, jj * (TILE // BLOCK) + hb]
                rows = slice(kb * BLOCK, (kb + 1) * BLOCK)
                cols = slice(hb * BLOCK, (hb + 1) * BLOCK)
                sub = w_ref[rows, cols]
                w_scr[rows, cols] = jnp.where(k == 0, jnp.zeros_like(sub), sub)

    @pl.when(j < n_half)
    def _():
        build(gw_ref, gk_ref, j)

    @pl.when(j >= n_half)
    def _():
        build(uw_ref, uk_ref, j - n_half)

    o_ref[...] = jnp.dot(x_ref[...], w_scr[...], preferred_element_type=jnp.float32)


def gate_up(x, gw, uw, gk, uk):
    t, f = x.shape
    h = gw.shape[1]
    n_half = h // TILE
    n_feat = f // BLOCK
    grid_spec = pltpu.PrefetchScalarGridSpec(
        num_scalar_prefetch=2,
        grid=(2 * n_half,),
        in_specs=[
            pl.BlockSpec((t, f), lambda j, gk, uk: (0, 0)),
            pl.BlockSpec((f, TILE), lambda j, gk, uk: (0, jnp.minimum(j, n_half - 1))),
            pl.BlockSpec((f, TILE), lambda j, gk, uk: (0, jnp.maximum(j - n_half, 0))),
        ],
        out_specs=pl.BlockSpec((t, TILE), lambda j, gk, uk: (0, j)),
        scratch_shapes=[pltpu.VMEM((f, TILE), x.dtype)],
    )
    return pl.pallas_call(
        functools.partial(_gate_up_kernel, n_half, n_feat),
        grid_spec=grid_spec,
        out_shape=jax.ShapeDtypeStruct((t, 2 * h), jnp.float32),
        compiler_params=pltpu.CompilerParams(dimension_semantics=("arbitrary",)),
        cost_estimate=pl.CostEstimate(
            flops=2 * t * f * 2 * h, transcendentals=0,
            bytes_accessed=2 * (t * f + 2 * f * h) + 4 * t * 2 * h,
        ),
    )(gk, uk, x, gw, uw)

ROW = ("z", "x_hi")
COL = ("x_lo", "y", "core")


def expand(weight, keep):
    nrow, ncol = keep.shape
    rows, cols = weight.shape
    masked = (
        weight.reshape(nrow, rows // nrow, ncol, cols // ncol)
        * keep.astype(jnp.bfloat16)[:, None, :, None]
    )
    return masked.reshape(rows, cols)


def shift(x, k, n):
    return lax.ppermute(x, ROW, [(i, (i + k) % n) for i in range(n)])


def on_device(tokens, gate_weight, up_weight, down_weight, gate_keep, up_keep, down_keep):
    n = lax.axis_size(ROW)
    hidden_cols = gate_weight.shape[1]
    features = jnp.concatenate([tokens] + [shift(tokens, k, n) for k in range(1, n)], axis=0)
    pair = gate_up(features, gate_weight, up_weight, gate_keep, up_keep)
    summed = lax.psum_scatter(pair, COL, scatter_dimension=0, tiled=True)
    hidden = (jax.nn.silu(summed[:, :hidden_cols]) * summed[:, hidden_cols:]).astype(jnp.bfloat16)
    hidden_all = lax.all_gather(hidden, COL, axis=0, tiled=True)
    partial_out = jnp.dot(
        hidden_all, expand(down_weight, down_keep), preferred_element_type=jnp.float32
    )
    t = tokens.shape[0]
    total = partial_out[:t]
    for k in range(1, n):
        total = total + shift(partial_out[k * t:(k + 1) * t], -k, n)
    return total.astype(jnp.bfloat16)


def solution(mesh):
    fine = Mesh(mesh.devices.reshape(4, 2, 2, 4, 2), ROW + COL)
    placed = (
        P(ROW, COL),
        P(COL, ROW),
        P(COL, ROW),
        P(ROW, COL),
        P(COL, ROW),
        P(COL, ROW),
        P(ROW, COL),
    )
    return jax.shard_map(
        on_device, mesh=fine, in_specs=placed, out_specs=P(ROW, COL), check_vma=False
    )
```

```python
import functools

import jax
import jax.numpy as jnp
from jax import lax
from jax.experimental import pallas as pl
from jax.experimental.pallas import tpu as pltpu
from jax.sharding import Mesh
from jax.sharding import PartitionSpec as P

BLOCK = 128
TILE = 1792


def _gate_up_kernel(n_half, n_feat, gk_ref, uk_ref, x_ref, gw_ref, uw_ref, o_ref, w_scr):
    j = pl.program_id(0)

    def build(w_ref, k_ref, jj):
        for kb in range(n_feat):
            for hb in range(TILE // BLOCK):
                k = k_ref[kb, jj * (TILE // BLOCK) + hb]
                rows = slice(kb * BLOCK, (kb + 1) * BLOCK)
                cols = slice(hb * BLOCK, (hb + 1) * BLOCK)
                sub = w_ref[rows, cols]
                w_scr[rows, cols] = jnp.where(k == 0, jnp.zeros_like(sub), sub)

    @pl.when(j < n_half)
    def _():
        build(gw_ref, gk_ref, j)

    @pl.when(j >= n_half)
    def _():
        build(uw_ref, uk_ref, j - n_half)

    o_ref[...] = jnp.dot(x_ref[...], w_scr[...], preferred_element_type=jnp.float32)


def gate_up(x, gw, uw, gk, uk):
    t, f = x.shape
    h = gw.shape[1]
    n_half = h // TILE
    n_feat = f // BLOCK
    grid_spec = pltpu.PrefetchScalarGridSpec(
        num_scalar_prefetch=2,
        grid=(2 * n_half,),
        in_specs=[
            pl.BlockSpec((t, f), lambda j, gk, uk: (0, 0)),
            pl.BlockSpec((f, TILE), lambda j, gk, uk: (0, jnp.minimum(j, n_half - 1))),
            pl.BlockSpec((f, TILE), lambda j, gk, uk: (0, jnp.maximum(j - n_half, 0))),
        ],
        out_specs=pl.BlockSpec((t, TILE), lambda j, gk, uk: (0, j)),
        scratch_shapes=[pltpu.VMEM((f, TILE), x.dtype)],
    )
    return pl.pallas_call(
        functools.partial(_gate_up_kernel, n_half, n_feat),
        grid_spec=grid_spec,
        out_shape=jax.ShapeDtypeStruct((t, 2 * h), jnp.float32),
        compiler_params=pltpu.CompilerParams(dimension_semantics=("arbitrary",)),
        cost_estimate=pl.CostEstimate(
            flops=2 * t * f * 2 * h, transcendentals=0,
            bytes_accessed=2 * (t * f + 2 * f * h) + 4 * t * 2 * h,
        ),
    )(gk, uk, x, gw, uw)

ROW = ("z", "x_hi")
COL = ("x_lo", "y", "core")


def expand(weight, keep):
    nrow, ncol = keep.shape
    rows, cols = weight.shape
    masked = (
        weight.reshape(nrow, rows // nrow, ncol, cols // ncol)
        * keep.astype(jnp.bfloat16)[:, None, :, None]
    )
    return masked.reshape(rows, cols)


def shift(x, k, n):
    return lax.ppermute(x, ROW, [(i, (i + k) % n) for i in range(n)])


def on_device(tokens, gate_weight, up_weight, down_weight, gate_keep, up_keep, down_keep):
    n = lax.axis_size(ROW)
    hidden_cols = gate_weight.shape[1]
    features = jnp.concatenate([tokens] + [shift(tokens, k, n) for k in range(1, n)], axis=0)
    pair = gate_up(features, gate_weight, up_weight, gate_keep, up_keep)
    summed = lax.psum_scatter(pair, COL, scatter_dimension=0, tiled=True)
    hidden = (jax.nn.silu(summed[:, :hidden_cols]) * summed[:, hidden_cols:]).astype(jnp.bfloat16)
    hidden_all = lax.all_gather(hidden, COL, axis=0, tiled=True)
    partial_out = jnp.dot(
        hidden_all, expand(down_weight, down_keep), preferred_element_type=jnp.float32
    )
    t = tokens.shape[0]
    total = partial_out[:t]
    for k in range(1, n):
        total = total + shift(partial_out[k * t:(k + 1) * t], -k, n)
    return total.astype(jnp.bfloat16)


def solution(mesh):
    fine = Mesh(mesh.devices.reshape(4, 2, 2, 4, 2), ROW + COL)
    placed = (
        P(ROW, COL),
        P(COL, ROW),
        P(COL, ROW),
        P(ROW, COL),
        P(COL, ROW),
        P(COL, ROW),
        P(ROW, COL),
    )
    return jax.shard_map(
        on_device, mesh=fine, in_specs=placed, out_specs=P(ROW, COL), check_vma=False
    )
```

```python
import functools

import jax
import jax.numpy as jnp
from jax import lax
from jax.experimental import pallas as pl
from jax.experimental.pallas import tpu as pltpu
from jax.sharding import Mesh
from jax.sharding import PartitionSpec as P

BLOCK = 128
TILE = 1792


def _gate_up_kernel(n_half, n_feat, gk_ref, uk_ref, x_ref, gw_ref, uw_ref, o_ref, w_scr):
    j = pl.program_id(0)

    def build(w_ref, k_ref, jj):
        for kb in range(n_feat):
            for hb in range(TILE // BLOCK):
                k = k_ref[kb, jj * (TILE // BLOCK) + hb]
                rows = slice(kb * BLOCK, (kb + 1) * BLOCK)
                cols = slice(hb * BLOCK, (hb + 1) * BLOCK)
                sub = w_ref[rows, cols]
                w_scr[rows, cols] = jnp.where(k == 0, jnp.zeros_like(sub), sub)

    @pl.when(j < n_half)
    def _():
        build(gw_ref, gk_ref, j)

    @pl.when(j >= n_half)
    def _():
        build(uw_ref, uk_ref, j - n_half)

    o_ref[...] = jnp.dot(x_ref[...], w_scr[...], preferred_element_type=jnp.float32)


def gate_up(x, gw, uw, gk, uk):
    t, f = x.shape
    h = gw.shape[1]
    n_half = h // TILE
    n_feat = f // BLOCK
    grid_spec = pltpu.PrefetchScalarGridSpec(
        num_scalar_prefetch=2,
        grid=(2 * n_half,),
        in_specs=[
            pl.BlockSpec((t, f), lambda j, gk, uk: (0, 0)),
            pl.BlockSpec((f, TILE), lambda j, gk, uk: (0, jnp.minimum(j, n_half - 1))),
            pl.BlockSpec((f, TILE), lambda j, gk, uk: (0, jnp.maximum(j - n_half, 0))),
        ],
        out_specs=pl.BlockSpec((t, TILE), lambda j, gk, uk: (0, j)),
        scratch_shapes=[pltpu.VMEM((f, TILE), x.dtype)],
    )
    return pl.pallas_call(
        functools.partial(_gate_up_kernel, n_half, n_feat),
        grid_spec=grid_spec,
        out_shape=jax.ShapeDtypeStruct((t, 2 * h), jnp.float32),
        compiler_params=pltpu.CompilerParams(dimension_semantics=("arbitrary",)),
        cost_estimate=pl.CostEstimate(
            flops=2 * t * f * 2 * h, transcendentals=0,
            bytes_accessed=2 * (t * f + 2 * f * h) + 4 * t * 2 * h,
        ),
    )(gk, uk, x, gw, uw)

ROW = ("z", "x_hi")
COL = ("x_lo", "y", "core")


def expand(weight, keep):
    nrow, ncol = keep.shape
    rows, cols = weight.shape
    masked = (
        weight.reshape(nrow, rows // nrow, ncol, cols // ncol)
        * keep.astype(jnp.bfloat16)[:, None, :, None]
    )
    return masked.reshape(rows, cols)


def partner(x, mask, n):
    return lax.ppermute(x, ROW, [(i, i ^ mask) for i in range(n)])


def row_masks(n):
    masks = [1 << b for b in range(n.bit_length() - 1)]
    if 2 in masks:
        masks.remove(2)
        masks.append(2)
    return masks


def on_device(tokens, gate_weight, up_weight, down_weight, gate_keep, up_keep, down_keep):
    n = lax.axis_size(ROW)
    hidden_cols = gate_weight.shape[1]
    masks = row_masks(n)
    features = tokens
    for mask in masks:
        features = jnp.concatenate([features, partner(features, mask, n)], axis=0)
    pair = gate_up(features, gate_weight, up_weight, gate_keep, up_keep)
    summed = lax.psum_scatter(pair, COL, scatter_dimension=0, tiled=True)
    hidden = (jax.nn.silu(summed[:, :hidden_cols]) * summed[:, hidden_cols:]).astype(jnp.bfloat16)
    hidden_all = lax.all_gather(hidden, COL, axis=0, tiled=True)
    partial_out = jnp.dot(
        hidden_all, expand(down_weight, down_keep), preferred_element_type=jnp.float32
    )
    total = partial_out
    for mask in reversed(masks):
        half = total.shape[0] // 2
        total = total[:half] + partner(total[half:], mask, n)
    return total.astype(jnp.bfloat16)


def solution(mesh):
    fine = Mesh(mesh.devices.reshape(4, 2, 2, 4, 2), ROW + COL)
    placed = (
        P(ROW, COL),
        P(COL, ROW),
        P(COL, ROW),
        P(ROW, COL),
        P(COL, ROW),
        P(COL, ROW),
        P(ROW, COL),
    )
    return jax.shard_map(
        on_device, mesh=fine, in_specs=placed, out_specs=P(ROW, COL), check_vma=False
    )
```

```python
import functools

import jax
import jax.numpy as jnp
from jax import lax
from jax.experimental import pallas as pl
from jax.experimental.pallas import tpu as pltpu
from jax.sharding import Mesh
from jax.sharding import PartitionSpec as P

BLOCK = 128
TILE = 1792


def _gate_up_kernel(part, n_feat, gk_ref, uk_ref, x_ref, gw_ref, uw_ref, o_ref, w_scr):
    j = pl.program_id(0)

    def build(w_ref, k_ref):
        for kb in range(n_feat):
            for hb in range(TILE // BLOCK):
                k = k_ref[kb, part * (TILE // BLOCK) + hb]
                rows = slice(kb * BLOCK, (kb + 1) * BLOCK)
                cols = slice(hb * BLOCK, (hb + 1) * BLOCK)
                sub = w_ref[rows, cols]
                w_scr[rows, cols] = jnp.where(k == 0, jnp.zeros_like(sub), sub)

    @pl.when(j == 0)
    def _():
        build(gw_ref, gk_ref)

    @pl.when(j == 1)
    def _():
        build(uw_ref, uk_ref)

    o_ref[...] = jnp.dot(x_ref[...], w_scr[...], preferred_element_type=jnp.float32)


def gate_up(x, gw, uw, gk, uk, part):
    t, f = x.shape
    n_feat = f // BLOCK
    grid_spec = pltpu.PrefetchScalarGridSpec(
        num_scalar_prefetch=2,
        grid=(2,),
        in_specs=[
            pl.BlockSpec((t, f), lambda j, gk, uk: (0, 0)),
            pl.BlockSpec((f, TILE), lambda j, gk, uk: (0, part)),
            pl.BlockSpec((f, TILE), lambda j, gk, uk: (0, part)),
        ],
        out_specs=pl.BlockSpec((t, TILE), lambda j, gk, uk: (0, j)),
        scratch_shapes=[pltpu.VMEM((f, TILE), x.dtype)],
    )
    return pl.pallas_call(
        functools.partial(_gate_up_kernel, part, n_feat),
        grid_spec=grid_spec,
        out_shape=jax.ShapeDtypeStruct((t, 2 * TILE), jnp.float32),
        compiler_params=pltpu.CompilerParams(dimension_semantics=("arbitrary",)),
        cost_estimate=pl.CostEstimate(
            flops=2 * t * f * 2 * TILE, transcendentals=0,
            bytes_accessed=2 * (t * f + 2 * f * TILE) + 4 * t * 2 * TILE,
        ),
    )(gk, uk, x, gw, uw)


ROW = ("z", "x_hi")
COL = ("x_lo", "y", "core")


def expand(weight, keep):
    nrow, ncol = keep.shape
    rows, cols = weight.shape
    masked = (
        weight.reshape(nrow, rows // nrow, ncol, cols // ncol)
        * keep.astype(jnp.bfloat16)[:, None, :, None]
    )
    return masked.reshape(rows, cols)


def shift(x, k, n):
    return lax.ppermute(x, ROW, [(i, (i + k) % n) for i in range(n)])


def on_device(tokens, gate_weight, up_weight, down_weight, gate_keep, up_keep, down_keep):
    n = lax.axis_size(ROW)
    hidden_cols = gate_weight.shape[1]
    features = jnp.concatenate([tokens] + [shift(tokens, k, n) for k in range(1, n)], axis=0)
    hidden_parts = []
    for part in range(hidden_cols // TILE):
        pair = gate_up(features, gate_weight, up_weight, gate_keep, up_keep, part)
        summed = lax.psum_scatter(pair, COL, scatter_dimension=0, tiled=True)
        hidden_parts.append(
            (jax.nn.silu(summed[:, :TILE]) * summed[:, TILE:]).astype(jnp.bfloat16)
        )
    hidden = jnp.concatenate(hidden_parts, axis=1)
    hidden_all = lax.all_gather(hidden, COL, axis=0, tiled=True)
    partial_out = jnp.dot(
        hidden_all, expand(down_weight, down_keep), preferred_element_type=jnp.float32
    )
    t = tokens.shape[0]
    total = partial_out[:t]
    for k in range(1, n):
        total = total + shift(partial_out[k * t:(k + 1) * t], -k, n)
    return total.astype(jnp.bfloat16)


def solution(mesh):
    fine = Mesh(mesh.devices.reshape(4, 2, 2, 4, 2), ROW + COL)
    placed = (
        P(ROW, COL),
        P(COL, ROW),
        P(COL, ROW),
        P(ROW, COL),
        P(COL, ROW),
        P(COL, ROW),
        P(ROW, COL),
    )
    return jax.shard_map(
        on_device, mesh=fine, in_specs=placed, out_specs=P(ROW, COL), check_vma=False
    )
```

```python
import functools

import jax
import jax.numpy as jnp
from jax import lax
from jax.experimental import pallas as pl
from jax.experimental.pallas import tpu as pltpu
from jax.sharding import Mesh
from jax.sharding import PartitionSpec as P

BLOCK = 128
TILE = 1792


def _gate_up_kernel(n_half, n_feat, gk_ref, uk_ref, x_ref, gw_ref, uw_ref, o_ref, w_scr):
    j = pl.program_id(0)

    def build(w_ref, k_ref, jj):
        for kb in range(n_feat):
            for hb in range(TILE // BLOCK):
                k = k_ref[kb, jj * (TILE // BLOCK) + hb]
                rows = slice(kb * BLOCK, (kb + 1) * BLOCK)
                cols = slice(hb * BLOCK, (hb + 1) * BLOCK)
                sub = w_ref[rows, cols]
                w_scr[rows, cols] = jnp.where(k == 0, jnp.zeros_like(sub), sub)

    @pl.when(j < n_half)
    def _():
        build(gw_ref, gk_ref, j)

    @pl.when(j >= n_half)
    def _():
        build(uw_ref, uk_ref, j - n_half)

    o_ref[...] = jnp.dot(x_ref[...], w_scr[...], preferred_element_type=jnp.float32)


def gate_up(x, gw, uw, gk, uk):
    t, f = x.shape
    h = gw.shape[1]
    n_half = h // TILE
    n_feat = f // BLOCK
    grid_spec = pltpu.PrefetchScalarGridSpec(
        num_scalar_prefetch=2,
        grid=(2 * n_half,),
        in_specs=[
            pl.BlockSpec((t, f), lambda j, gk, uk: (0, 0)),
            pl.BlockSpec((f, TILE), lambda j, gk, uk: (0, jnp.minimum(j, n_half - 1))),
            pl.BlockSpec((f, TILE), lambda j, gk, uk: (0, jnp.maximum(j - n_half, 0))),
        ],
        out_specs=pl.BlockSpec((t, TILE), lambda j, gk, uk: (0, j)),
        scratch_shapes=[pltpu.VMEM((f, TILE), x.dtype)],
    )
    return pl.pallas_call(
        functools.partial(_gate_up_kernel, n_half, n_feat),
        grid_spec=grid_spec,
        out_shape=jax.ShapeDtypeStruct((t, 2 * h), jnp.float32),
        compiler_params=pltpu.CompilerParams(dimension_semantics=("arbitrary",)),
        cost_estimate=pl.CostEstimate(
            flops=2 * t * f * 2 * h, transcendentals=0,
            bytes_accessed=2 * (t * f + 2 * f * h) + 4 * t * 2 * h,
        ),
    )(gk, uk, x, gw, uw)

ROW = ("z", "x_hi")
COL = ("x_lo", "y", "core")


def expand(weight, keep):
    nrow, ncol = keep.shape
    rows, cols = weight.shape
    masked = (
        weight.reshape(nrow, rows // nrow, ncol, cols // ncol)
        * keep.astype(jnp.bfloat16)[:, None, :, None]
    )
    return masked.reshape(rows, cols)


def permute(x, dest):
    return lax.ppermute(x, ROW, [(i, dest(i)) for i in range(lax.axis_size(ROW))])


def z_shift(x, s, n_hi):
    n_z = lax.axis_size(ROW) // n_hi
    return permute(x, lambda i: ((i // n_hi + s) % n_z) * n_hi + i % n_hi)


def hi_swap(x):
    return permute(x, lambda i: i ^ 1)


def on_device(tokens, gate_weight, up_weight, down_weight, gate_keep, up_keep, down_keep):
    n_hi = lax.axis_size("x_hi")
    n_z = lax.axis_size("z")
    hidden_cols = gate_weight.shape[1]
    pair_rows = jnp.concatenate([tokens, hi_swap(tokens)], axis=0)
    features = jnp.concatenate(
        [pair_rows] + [z_shift(pair_rows, s, n_hi) for s in range(1, n_z)], axis=0
    )
    pair = gate_up(features, gate_weight, up_weight, gate_keep, up_keep)
    summed = lax.psum_scatter(pair, COL, scatter_dimension=0, tiled=True)
    hidden = (jax.nn.silu(summed[:, :hidden_cols]) * summed[:, hidden_cols:]).astype(jnp.bfloat16)
    hidden_all = lax.all_gather(hidden, COL, axis=0, tiled=True)
    partial_out = jnp.dot(
        hidden_all, expand(down_weight, down_keep), preferred_element_type=jnp.float32
    )
    t2 = 2 * tokens.shape[0]
    pair_sum = partial_out[:t2]
    for s in range(1, n_z):
        pair_sum = pair_sum + z_shift(partial_out[s * t2:(s + 1) * t2], -s, n_hi)
    t = tokens.shape[0]
    return (pair_sum[:t] + hi_swap(pair_sum[t:])).astype(jnp.bfloat16)


def solution(mesh):
    fine = Mesh(mesh.devices.reshape(4, 2, 2, 4, 2), ROW + COL)
    placed = (
        P(ROW, COL),
        P(COL, ROW),
        P(COL, ROW),
        P(ROW, COL),
        P(COL, ROW),
        P(COL, ROW),
        P(ROW, COL),
    )
    return jax.shard_map(
        on_device, mesh=fine, in_specs=placed, out_specs=P(ROW, COL), check_vma=False
    )
```

```python
import functools

import jax
import jax.numpy as jnp
from jax import lax
from jax.experimental import pallas as pl
from jax.experimental.pallas import tpu as pltpu
from jax.sharding import Mesh
from jax.sharding import PartitionSpec as P

BLOCK = 128
TILE = 1792


def _gate_up_kernel(n_half, n_feat, gk_ref, uk_ref, x_ref, gw_ref, uw_ref, o_ref, w_scr):
    j = pl.program_id(0)

    def build(w_ref, k_ref, jj):
        for kb in range(n_feat):
            for hb in range(TILE // BLOCK):
                k = k_ref[kb, jj * (TILE // BLOCK) + hb]
                rows = slice(kb * BLOCK, (kb + 1) * BLOCK)
                cols = slice(hb * BLOCK, (hb + 1) * BLOCK)
                sub = w_ref[rows, cols]
                w_scr[rows, cols] = jnp.where(k == 0, jnp.zeros_like(sub), sub)

    @pl.when(j < n_half)
    def _():
        build(gw_ref, gk_ref, j)

    @pl.when(j >= n_half)
    def _():
        build(uw_ref, uk_ref, j - n_half)

    o_ref[...] = jnp.dot(x_ref[...], w_scr[...], preferred_element_type=jnp.float32)


def gate_up(x, gw, uw, gk, uk):
    t, f = x.shape
    h = gw.shape[1]
    n_half = h // TILE
    n_feat = f // BLOCK
    grid_spec = pltpu.PrefetchScalarGridSpec(
        num_scalar_prefetch=2,
        grid=(2 * n_half,),
        in_specs=[
            pl.BlockSpec((t, f), lambda j, gk, uk: (0, 0)),
            pl.BlockSpec((f, TILE), lambda j, gk, uk: (0, jnp.minimum(j, n_half - 1))),
            pl.BlockSpec((f, TILE), lambda j, gk, uk: (0, jnp.maximum(j - n_half, 0))),
        ],
        out_specs=pl.BlockSpec((t, TILE), lambda j, gk, uk: (0, j)),
        scratch_shapes=[pltpu.VMEM((f, TILE), x.dtype)],
    )
    return pl.pallas_call(
        functools.partial(_gate_up_kernel, n_half, n_feat),
        grid_spec=grid_spec,
        out_shape=jax.ShapeDtypeStruct((t, 2 * h), jnp.float32),
        compiler_params=pltpu.CompilerParams(dimension_semantics=("arbitrary",)),
        cost_estimate=pl.CostEstimate(
            flops=2 * t * f * 2 * h, transcendentals=0,
            bytes_accessed=2 * (t * f + 2 * f * h) + 4 * t * 2 * h,
        ),
    )(gk, uk, x, gw, uw)

ROW = ("z", "x_hi")
COL = ("x_lo", "y", "core")


def expand(weight, keep):
    nrow, ncol = keep.shape
    rows, cols = weight.shape
    masked = (
        weight.reshape(nrow, rows // nrow, ncol, cols // ncol)
        * keep.astype(jnp.bfloat16)[:, None, :, None]
    )
    return masked.reshape(rows, cols)


def permute(x, dest):
    return lax.ppermute(x, ROW, [(i, dest(i)) for i in range(lax.axis_size(ROW))])


def z_shift(x, s, n_hi):
    n_z = lax.axis_size(ROW) // n_hi
    return permute(x, lambda i: ((i // n_hi + s) % n_z) * n_hi + i % n_hi)


def hi_swap(x):
    return permute(x, lambda i: i ^ 1)


def on_device(tokens, gate_weight, up_weight, down_weight, gate_keep, up_keep, down_keep):
    n_hi = lax.axis_size("x_hi")
    n_z = lax.axis_size("z")
    hidden_cols = gate_weight.shape[1]
    pair_rows = jnp.concatenate([tokens, hi_swap(tokens)], axis=0)
    features = jnp.concatenate(
        [pair_rows] + [z_shift(pair_rows, s, n_hi) for s in range(1, n_z)], axis=0
    )
    pair = gate_up(features, gate_weight, up_weight, gate_keep, up_keep)
    summed = lax.psum_scatter(pair, COL, scatter_dimension=0, tiled=True)
    hidden = (jax.nn.silu(summed[:, :hidden_cols]) * summed[:, hidden_cols:]).astype(jnp.bfloat16)
    hidden_all = lax.all_gather(hidden, COL, axis=0, tiled=True)
    partial_out = jnp.dot(
        hidden_all, expand(down_weight, down_keep), preferred_element_type=jnp.float32
    )
    t = tokens.shape[0]
    total = partial_out[:t]
    for s in range(n_z):
        for i in range(n_hi):
            if s == 0 and i == 0:
                continue
            b = s * n_hi + i
            total = total + permute(
                partial_out[b * t:(b + 1) * t],
                lambda L, s=s, i=i: ((L // n_hi - s) % n_z) * n_hi + ((L % n_hi) ^ i),
            )
    return total.astype(jnp.bfloat16)


def solution(mesh):
    fine = Mesh(mesh.devices.reshape(4, 2, 2, 4, 2), ROW + COL)
    placed = (
        P(ROW, COL),
        P(COL, ROW),
        P(COL, ROW),
        P(ROW, COL),
        P(COL, ROW),
        P(COL, ROW),
        P(ROW, COL),
    )
    return jax.shard_map(
        on_device, mesh=fine, in_specs=placed, out_specs=P(ROW, COL), check_vma=False
    )
```

```python
import functools

import jax
import jax.numpy as jnp
from jax import lax
from jax.experimental import pallas as pl
from jax.experimental.pallas import tpu as pltpu
from jax.sharding import Mesh
from jax.sharding import PartitionSpec as P

BLOCK = 128
TILE = 1792


def _gate_up_kernel(n_half, n_feat, gk_ref, uk_ref, x_ref, gw_ref, uw_ref, o_ref, w_scr):
    j = pl.program_id(0)

    def build(w_ref, k_ref, jj):
        for kb in range(n_feat):
            for hb in range(TILE // BLOCK):
                k = k_ref[kb, jj * (TILE // BLOCK) + hb]
                rows = slice(kb * BLOCK, (kb + 1) * BLOCK)
                cols = slice(hb * BLOCK, (hb + 1) * BLOCK)
                sub = w_ref[rows, cols]
                w_scr[rows, cols] = jnp.where(k == 0, jnp.zeros_like(sub), sub)

    @pl.when(j < n_half)
    def _():
        build(gw_ref, gk_ref, j)

    @pl.when(j >= n_half)
    def _():
        build(uw_ref, uk_ref, j - n_half)

    o_ref[...] = jnp.dot(x_ref[...], w_scr[...], preferred_element_type=jnp.float32)


def gate_up(x, gw, uw, gk, uk):
    t, f = x.shape
    h = gw.shape[1]
    n_half = h // TILE
    n_feat = f // BLOCK
    grid_spec = pltpu.PrefetchScalarGridSpec(
        num_scalar_prefetch=2,
        grid=(2 * n_half,),
        in_specs=[
            pl.BlockSpec((t, f), lambda j, gk, uk: (0, 0)),
            pl.BlockSpec((f, TILE), lambda j, gk, uk: (0, jnp.minimum(j, n_half - 1))),
            pl.BlockSpec((f, TILE), lambda j, gk, uk: (0, jnp.maximum(j - n_half, 0))),
        ],
        out_specs=pl.BlockSpec((t, TILE), lambda j, gk, uk: (0, j)),
        scratch_shapes=[pltpu.VMEM((f, TILE), x.dtype)],
    )
    return pl.pallas_call(
        functools.partial(_gate_up_kernel, n_half, n_feat),
        grid_spec=grid_spec,
        out_shape=jax.ShapeDtypeStruct((t, 2 * h), jnp.float32),
        compiler_params=pltpu.CompilerParams(dimension_semantics=("arbitrary",)),
        cost_estimate=pl.CostEstimate(
            flops=2 * t * f * 2 * h, transcendentals=0,
            bytes_accessed=2 * (t * f + 2 * f * h) + 4 * t * 2 * h,
        ),
    )(gk, uk, x, gw, uw)

ROW = ("z", "x_hi")
COL = ("x_lo", "y", "core")


def expand(weight, keep):
    nrow, ncol = keep.shape
    rows, cols = weight.shape
    masked = (
        weight.reshape(nrow, rows // nrow, ncol, cols // ncol)
        * keep.astype(jnp.bfloat16)[:, None, :, None]
    )
    return masked.reshape(rows, cols)


def permute(x, dest):
    return lax.ppermute(x, ROW, [(i, dest(i)) for i in range(lax.axis_size(ROW))])


def z_shift(x, s, n_hi):
    n_z = lax.axis_size(ROW) // n_hi
    return permute(x, lambda i: ((i // n_hi + s) % n_z) * n_hi + i % n_hi)


def hi_swap(x):
    return permute(x, lambda i: i ^ 1)


def on_device(tokens, gate_weight, up_weight, down_weight, gate_keep, up_keep, down_keep):
    n_hi = lax.axis_size("x_hi")
    n_z = lax.axis_size("z")
    hidden_cols = gate_weight.shape[1]
    pair_rows = jnp.concatenate([tokens, hi_swap(tokens)], axis=0)
    features = jnp.concatenate(
        [pair_rows] + [z_shift(pair_rows, s, n_hi) for s in range(1, n_z)], axis=0
    )
    pair = gate_up(features, gate_weight, up_weight, gate_keep, up_keep)
    summed = lax.psum_scatter(pair, COL, scatter_dimension=0, tiled=True)
    down_mat = expand(down_weight, down_keep)
    summed, down_mat = lax.optimization_barrier((summed, down_mat))
    hidden = (jax.nn.silu(summed[:, :hidden_cols]) * summed[:, hidden_cols:]).astype(jnp.bfloat16)
    hidden_all = lax.all_gather(hidden, COL, axis=0, tiled=True)
    partial_out = jnp.dot(
        hidden_all, down_mat, preferred_element_type=jnp.float32
    )
    t = tokens.shape[0]
    total = partial_out[:t]
    for s in range(n_z):
        for i in range(n_hi):
            if s == 0 and i == 0:
                continue
            b = s * n_hi + i
            total = total + permute(
                partial_out[b * t:(b + 1) * t],
                lambda L, s=s, i=i: ((L // n_hi - s) % n_z) * n_hi + ((L % n_hi) ^ i),
            )
    return total.astype(jnp.bfloat16)


def solution(mesh):
    fine = Mesh(mesh.devices.reshape(4, 2, 2, 4, 2), ROW + COL)
    placed = (
        P(ROW, COL),
        P(COL, ROW),
        P(COL, ROW),
        P(ROW, COL),
        P(COL, ROW),
        P(COL, ROW),
        P(ROW, COL),
    )
    return jax.shard_map(
        on_device, mesh=fine, in_specs=placed, out_specs=P(ROW, COL), check_vma=False
    )
```

```python
import functools

import jax
import jax.numpy as jnp
from jax import lax
from jax.experimental import pallas as pl
from jax.experimental.pallas import tpu as pltpu
from jax.sharding import Mesh
from jax.sharding import PartitionSpec as P

BLOCK = 128
TILE = 1792


def _gate_up_kernel(n_half, n_feat, gk_ref, uk_ref, x_ref, gw_ref, uw_ref, o_ref, w_scr):
    j = pl.program_id(0)

    def build(w_ref, k_ref, jj):
        for kb in range(n_feat):
            for hb in range(TILE // BLOCK):
                k = k_ref[kb, jj * (TILE // BLOCK) + hb]
                rows = slice(kb * BLOCK, (kb + 1) * BLOCK)
                cols = slice(hb * BLOCK, (hb + 1) * BLOCK)
                sub = w_ref[rows, cols]
                w_scr[rows, cols] = jnp.where(k == 0, jnp.zeros_like(sub), sub)

    @pl.when(j < n_half)
    def _():
        build(gw_ref, gk_ref, j)

    @pl.when(j >= n_half)
    def _():
        build(uw_ref, uk_ref, j - n_half)

    o_ref[...] = jnp.dot(x_ref[...], w_scr[...], preferred_element_type=jnp.float32)


def gate_up(x, gw, uw, gk, uk):
    t, f = x.shape
    h = gw.shape[1]
    n_half = h // TILE
    n_feat = f // BLOCK
    grid_spec = pltpu.PrefetchScalarGridSpec(
        num_scalar_prefetch=2,
        grid=(2 * n_half,),
        in_specs=[
            pl.BlockSpec((t, f), lambda j, gk, uk: (0, 0)),
            pl.BlockSpec((f, TILE), lambda j, gk, uk: (0, jnp.minimum(j, n_half - 1))),
            pl.BlockSpec((f, TILE), lambda j, gk, uk: (0, jnp.maximum(j - n_half, 0))),
        ],
        out_specs=pl.BlockSpec((t, TILE), lambda j, gk, uk: (0, j)),
        scratch_shapes=[pltpu.VMEM((f, TILE), x.dtype)],
    )
    return pl.pallas_call(
        functools.partial(_gate_up_kernel, n_half, n_feat),
        grid_spec=grid_spec,
        out_shape=jax.ShapeDtypeStruct((t, 2 * h), jnp.float32),
        compiler_params=pltpu.CompilerParams(dimension_semantics=("arbitrary",)),
        cost_estimate=pl.CostEstimate(
            flops=2 * t * f * 2 * h, transcendentals=0,
            bytes_accessed=2 * (t * f + 2 * f * h) + 4 * t * 2 * h,
        ),
    )(gk, uk, x, gw, uw)

ROW = ("z", "x_hi")
COL = ("x_lo", "y", "core")


def expand(weight, keep):
    nrow, ncol = keep.shape
    rows, cols = weight.shape
    masked = (
        weight.reshape(nrow, rows // nrow, ncol, cols // ncol)
        * keep.astype(jnp.bfloat16)[:, None, :, None]
    )
    return masked.reshape(rows, cols)


def permute(x, dest):
    return lax.ppermute(x, ROW, [(i, dest(i)) for i in range(lax.axis_size(ROW))])


def z_shift(x, s, n_hi):
    n_z = lax.axis_size(ROW) // n_hi
    return permute(x, lambda i: ((i // n_hi + s) % n_z) * n_hi + i % n_hi)


def hi_swap(x):
    return permute(x, lambda i: i ^ 1)


def on_device(tokens, gate_weight, up_weight, down_weight, gate_keep, up_keep, down_keep):
    n_hi = lax.axis_size("x_hi")
    n_z = lax.axis_size("z")
    hidden_cols = gate_weight.shape[1]
    pair_rows = jnp.concatenate([tokens, hi_swap(tokens)], axis=0)
    features = jnp.concatenate(
        [pair_rows] + [z_shift(pair_rows, s, n_hi) for s in range(1, n_z)], axis=0
    )
    pair = gate_up(features, gate_weight, up_weight, gate_keep, up_keep)
    summed = lax.psum_scatter(pair, COL, scatter_dimension=0, tiled=True)
    down_mat = expand(down_weight, down_keep)
    summed, down_mat = lax.optimization_barrier((summed, down_mat))
    hidden = (jax.nn.silu(summed[:, :hidden_cols]) * summed[:, hidden_cols:]).astype(jnp.bfloat16)
    hidden_all = lax.all_gather(hidden, COL, axis=0, tiled=True)
    t = tokens.shape[0]

    def block(b):
        return jnp.dot(
            hidden_all[b * t:(b + 1) * t], down_mat, preferred_element_type=jnp.float32
        )

    total = None
    for s in range(n_z):
        for i in range(n_hi):
            if s == 0 and i == 0:
                continue
            b = s * n_hi + i
            sent = permute(
                block(b),
                lambda L, s=s, i=i: ((L // n_hi - s) % n_z) * n_hi + ((L % n_hi) ^ i),
            )
            total = sent if total is None else total + sent
    total = block(0) + total
    return total.astype(jnp.bfloat16)


def solution(mesh):
    fine = Mesh(mesh.devices.reshape(4, 2, 2, 4, 2), ROW + COL)
    placed = (
        P(ROW, COL),
        P(COL, ROW),
        P(COL, ROW),
        P(ROW, COL),
        P(COL, ROW),
        P(COL, ROW),
        P(ROW, COL),
    )
    return jax.shard_map(
        on_device, mesh=fine, in_specs=placed, out_specs=P(ROW, COL), check_vma=False
    )
```

```python
import functools

import jax
import jax.numpy as jnp
from jax import lax
from jax.experimental import pallas as pl
from jax.experimental.pallas import tpu as pltpu
from jax.sharding import Mesh
from jax.sharding import PartitionSpec as P

BLOCK = 128
TILE = 1792


def _gate_up_kernel(n_half, n_feat, gk_ref, uk_ref, x_ref, gw_ref, uw_ref, *refs):
    o_ref, w_scr = refs[-2:]
    j = pl.program_id(0)

    def build(w_ref, k_ref, jj):
        for kb in range(n_feat):
            for hb in range(TILE // BLOCK):
                k = k_ref[kb, jj * (TILE // BLOCK) + hb]
                rows = slice(kb * BLOCK, (kb + 1) * BLOCK)
                cols = slice(hb * BLOCK, (hb + 1) * BLOCK)
                sub = w_ref[rows, cols]
                w_scr[rows, cols] = jnp.where(k == 0, jnp.zeros_like(sub), sub)

    @pl.when(j < n_half)
    def _():
        build(gw_ref, gk_ref, j)

    @pl.when(j >= n_half)
    def _():
        build(uw_ref, uk_ref, j - n_half)

    o_ref[...] = jnp.dot(x_ref[...], w_scr[...], preferred_element_type=jnp.float32)


def gate_up(x, gw, uw, gk, uk, rows, row_block, into=None):
    t, f = x.shape
    h = gw.shape[1]
    n_half = h // TILE
    n_feat = f // BLOCK
    in_specs = [
        pl.BlockSpec((t, f), lambda j, gk, uk: (0, 0)),
        pl.BlockSpec((f, TILE), lambda j, gk, uk: (0, jnp.minimum(j, n_half - 1))),
        pl.BlockSpec((f, TILE), lambda j, gk, uk: (0, jnp.maximum(j - n_half, 0))),
    ]
    operands = [gk, uk, x, gw, uw]
    aliases = {}
    if into is not None:
        in_specs.append(pl.BlockSpec(memory_space=pl.ANY))
        aliases = {len(operands): 0}
        operands.append(into)
    grid_spec = pltpu.PrefetchScalarGridSpec(
        num_scalar_prefetch=2,
        grid=(2 * n_half,),
        in_specs=in_specs,
        out_specs=pl.BlockSpec((t, TILE), lambda j, gk, uk: (row_block, j)),
        scratch_shapes=[pltpu.VMEM((f, TILE), x.dtype)],
    )
    return pl.pallas_call(
        functools.partial(_gate_up_kernel, n_half, n_feat),
        grid_spec=grid_spec,
        out_shape=jax.ShapeDtypeStruct((rows, 2 * h), jnp.float32),
        input_output_aliases=aliases,
        compiler_params=pltpu.CompilerParams(dimension_semantics=("arbitrary",)),
        cost_estimate=pl.CostEstimate(
            flops=2 * t * f * 2 * h, transcendentals=0,
            bytes_accessed=2 * (t * f + 2 * f * h) + 4 * t * 2 * h,
        ),
    )(*operands)


ROW = ("z", "x_hi")
COL = ("x_lo", "y", "core")


def expand(weight, keep):
    nrow, ncol = keep.shape
    rows, cols = weight.shape
    masked = (
        weight.reshape(nrow, rows // nrow, ncol, cols // ncol)
        * keep.astype(jnp.bfloat16)[:, None, :, None]
    )
    return masked.reshape(rows, cols)


def permute(x, dest):
    return lax.ppermute(x, ROW, [(i, dest(i)) for i in range(lax.axis_size(ROW))])


def z_shift(x, s, n_hi):
    n_z = lax.axis_size(ROW) // n_hi
    return permute(x, lambda i: ((i // n_hi + s) % n_z) * n_hi + i % n_hi)


def hi_swap(x):
    return permute(x, lambda i: i ^ 1)


def on_device(tokens, gate_weight, up_weight, down_weight, gate_keep, up_keep, down_keep):
    n_hi = lax.axis_size("x_hi")
    n_z = lax.axis_size("z")
    hidden_cols = gate_weight.shape[1]
    pair_rows = jnp.concatenate([tokens, hi_swap(tokens)], axis=0)
    shifted = [z_shift(pair_rows, s, n_hi) for s in range(1, n_z)]
    features = jnp.concatenate([pair_rows] + shifted, axis=0)
    rows = features.shape[0]
    half = rows // 2
    pair = gate_up(features[:half], gate_weight, up_weight, gate_keep, up_keep, rows, 0)
    pair = gate_up(
        features[half:], gate_weight, up_weight, gate_keep, up_keep, rows, 1, into=pair
    )
    summed = lax.psum_scatter(pair, COL, scatter_dimension=0, tiled=True)
    down_mat = expand(down_weight, down_keep)
    summed, down_mat = lax.optimization_barrier((summed, down_mat))
    hidden = (jax.nn.silu(summed[:, :hidden_cols]) * summed[:, hidden_cols:]).astype(jnp.bfloat16)
    hidden_all = lax.all_gather(hidden, COL, axis=0, tiled=True)
    partial_out = jnp.dot(
        hidden_all, down_mat, preferred_element_type=jnp.float32
    )
    t = tokens.shape[0]
    total = partial_out[:t]
    for s in range(n_z):
        for i in range(n_hi):
            if s == 0 and i == 0:
                continue
            b = s * n_hi + i
            total = total + permute(
                partial_out[b * t:(b + 1) * t],
                lambda L, s=s, i=i: ((L // n_hi - s) % n_z) * n_hi + ((L % n_hi) ^ i),
            )
    return total.astype(jnp.bfloat16)


def solution(mesh):
    fine = Mesh(mesh.devices.reshape(4, 2, 2, 4, 2), ROW + COL)
    placed = (
        P(ROW, COL),
        P(COL, ROW),
        P(COL, ROW),
        P(ROW, COL),
        P(COL, ROW),
        P(COL, ROW),
        P(ROW, COL),
    )
    return jax.shard_map(
        on_device, mesh=fine, in_specs=placed, out_specs=P(ROW, COL), check_vma=False
    )
```

```python
import functools

import jax
import jax.numpy as jnp
from jax import lax
from jax.experimental import pallas as pl
from jax.experimental.pallas import tpu as pltpu
from jax.sharding import Mesh
from jax.sharding import PartitionSpec as P

BLOCK = 128
TILE = 1792


def _gate_up_kernel(n_half, n_feat, gk_ref, uk_ref, x_ref, gw_ref, uw_ref, o_ref, w_scr):
    j = pl.program_id(0)

    def build(w_ref, k_ref, jj):
        for kb in range(n_feat):
            for hb in range(TILE // BLOCK):
                k = k_ref[kb, jj * (TILE // BLOCK) + hb]
                rows = slice(kb * BLOCK, (kb + 1) * BLOCK)
                cols = slice(hb * BLOCK, (hb + 1) * BLOCK)
                sub = w_ref[rows, cols]
                w_scr[rows, cols] = jnp.where(k == 0, jnp.zeros_like(sub), sub)

    @pl.when(j < n_half)
    def _():
        build(gw_ref, gk_ref, j)

    @pl.when(j >= n_half)
    def _():
        build(uw_ref, uk_ref, j - n_half)

    o_ref[...] = jnp.dot(x_ref[...], w_scr[...], preferred_element_type=jnp.float32)


def gate_up(x, gw, uw, gk, uk):
    t, f = x.shape
    h = gw.shape[1]
    n_half = h // TILE
    n_feat = f // BLOCK
    grid_spec = pltpu.PrefetchScalarGridSpec(
        num_scalar_prefetch=2,
        grid=(2 * n_half,),
        in_specs=[
            pl.BlockSpec((t, f), lambda j, gk, uk: (0, 0)),
            pl.BlockSpec((f, TILE), lambda j, gk, uk: (0, jnp.minimum(j, n_half - 1))),
            pl.BlockSpec((f, TILE), lambda j, gk, uk: (0, jnp.maximum(j - n_half, 0))),
        ],
        out_specs=pl.BlockSpec((t, TILE), lambda j, gk, uk: (0, j)),
        scratch_shapes=[pltpu.VMEM((f, TILE), x.dtype)],
    )
    return pl.pallas_call(
        functools.partial(_gate_up_kernel, n_half, n_feat),
        grid_spec=grid_spec,
        out_shape=jax.ShapeDtypeStruct((t, 2 * h), jnp.float32),
        compiler_params=pltpu.CompilerParams(dimension_semantics=("arbitrary",)),
        cost_estimate=pl.CostEstimate(
            flops=2 * t * f * 2 * h, transcendentals=0,
            bytes_accessed=2 * (t * f + 2 * f * h) + 4 * t * 2 * h,
        ),
    )(gk, uk, x, gw, uw)

ROW = ("z", "x_hi")
COL = ("x_lo", "y", "core")


def expand(weight, keep):
    nrow, ncol = keep.shape
    rows, cols = weight.shape
    masked = (
        weight.reshape(nrow, rows // nrow, ncol, cols // ncol)
        * keep.astype(jnp.bfloat16)[:, None, :, None]
    )
    return masked.reshape(rows, cols)


def permute(x, dest):
    return lax.ppermute(x, ROW, [(i, dest(i)) for i in range(lax.axis_size(ROW))])


def z_shift(x, s, n_hi):
    n_z = lax.axis_size(ROW) // n_hi
    return permute(x, lambda i: ((i // n_hi + s) % n_z) * n_hi + i % n_hi)


def hi_swap(x):
    return permute(x, lambda i: i ^ 1)


def on_device(tokens, gate_weight, up_weight, down_weight, gate_keep, up_keep, down_keep):
    n_hi = lax.axis_size("x_hi")
    n_z = lax.axis_size("z")
    hidden_cols = gate_weight.shape[1]
    z_rows = jnp.concatenate(
        [tokens] + [z_shift(tokens, s, n_hi) for s in range(1, n_z)], axis=0
    )
    features = jnp.concatenate([z_rows, hi_swap(z_rows)], axis=0)
    pair = gate_up(features, gate_weight, up_weight, gate_keep, up_keep)
    summed = lax.psum_scatter(pair, COL, scatter_dimension=0, tiled=True)
    down_mat = expand(down_weight, down_keep)
    summed, down_mat = lax.optimization_barrier((summed, down_mat))
    hidden = (jax.nn.silu(summed[:, :hidden_cols]) * summed[:, hidden_cols:]).astype(jnp.bfloat16)
    hidden_all = lax.all_gather(hidden, COL, axis=0, tiled=True)
    partial_out = jnp.dot(
        hidden_all, down_mat, preferred_element_type=jnp.float32
    )
    t = tokens.shape[0]
    total = partial_out[:t]
    for s in range(n_z):
        for i in range(n_hi):
            if s == 0 and i == 0:
                continue
            b = i * n_z + s
            total = total + permute(
                partial_out[b * t:(b + 1) * t],
                lambda L, s=s, i=i: ((L // n_hi - s) % n_z) * n_hi + ((L % n_hi) ^ i),
            )
    return total.astype(jnp.bfloat16)


def solution(mesh):
    fine = Mesh(mesh.devices.reshape(4, 2, 2, 4, 2), ROW + COL)
    placed = (
        P(ROW, COL),
        P(COL, ROW),
        P(COL, ROW),
        P(ROW, COL),
        P(COL, ROW),
        P(COL, ROW),
        P(ROW, COL),
    )
    return jax.shard_map(
        on_device, mesh=fine, in_specs=placed, out_specs=P(ROW, COL), check_vma=False
    )
```
